512 devices in a mesh: prow: 16 (over x, y_lo, core), pcol: 32 (over z, y_hi).
Axes of the slice: x: 4, y: 4 (y_hi: 2, y_lo: 2; y = y_hi * 2 + y_lo), z: 16, core: 2. Of those that a mesh axis runs over, the one named last changes fastest.
Arguments:
- velocity_u: bfloat16 [128, 1024, 1024], P('prow', 'pcol'), may hold values from -6 to 6
- velocity_v: bfloat16 [128, 1024, 1024], P('prow', 'pcol'), may hold values from -6 to 6
- velocity_w: bfloat16 [128, 1024, 1024], P('prow', 'pcol'), may hold values from -6 to 6
- x_derivative: bfloat16 [1024, 1024], P('pcol'), may hold values from -2 to 2
- y_derivative: bfloat16 [128, 128], replicated, may hold values from -2 to 2
- z_derivative: bfloat16 [1024, 1024], P('prow'), may hold values from -2 to 2
Outputs:
- u_tendency: float32 [128, 1024, 1024], P('pcol', 'prow')
- divergence: float32 [1024, 1024, 128], P('pcol', 'prow')
The draws below stay inside these ranges and needn't reach their ends.
All inputs are finite; a program needn't handle non-finite values.
Results may differ from the reference program's by a relative error of at most 0.0018.
Values may be sent and summed in bfloat16 or wider, within the bound.
No kernel may reach another device: no remote copies, remote signals or barrier semaphores. Data moves between devices by JAX's collectives and lax.ppermute only.
A program may use at most 64 MiB of HBM per device.

```python
import math
import jax
import jax.numpy as jnp
from jax import lax

NX = 1024
NY = 128
NZ = 1024
N_PCOL = 32


def operator_draw(key, order, periodic, stretched):
    row_index = jnp.arange(order)[:, None]
    col_index = jnp.arange(order)[None, :]
    offset = col_index - row_index
    if periodic:
        offset = (offset + order // 2) % order - order // 2
    distance = jnp.abs(offset)
    sign_of = jnp.sign(offset).astype(jnp.float32)
    coefficient = jnp.where(distance == 1, 0.75, jnp.where(distance == 2, -0.15, jnp.where(distance == 3, 1.0 / 60.0, 0.0)))
    banded = sign_of * coefficient
    first_key, second_key = jax.random.split(key)
    random_part = jnp.clip(jax.random.normal(first_key, (order, order), jnp.float32), -4.0, 4.0)
    combined = banded + 0.4 / math.sqrt(order) * random_part
    if stretched:
        metric = jnp.exp(jax.random.uniform(second_key, (order, 1), jnp.float32, math.log(0.5), math.log(2.0)))
        combined = combined * metric
    return combined.astype(jnp.bfloat16)


def draw_x_derivative(key, part):
    return operator_draw(jax.random.fold_in(key, 11), NX, True, False)


def draw_y_derivative(key, part):
    return operator_draw(jax.random.fold_in(key, 12), NY, False, True)


def draw_z_derivative(key, part):
    return operator_draw(jax.random.fold_in(key, 13), NZ, True, False)


def shard_levels(own_key, extent, cuts, smallest, high):
    def one(axis_at, shards_of):
        draws = jax.random.uniform(jax.random.fold_in(jax.random.fold_in(own_key, 6), axis_at), (shards_of,), jnp.float32, smallest / len(cuts), high / len(cuts))
        return jnp.repeat(jnp.exp(draws), extent[axis_at] // shards_of).reshape((-1,) + (1,) * (len(extent) - axis_at - 1))

    level = one(*cuts[0])
    for cut in cuts[1:]:
        level = level * one(*cut)
    return level


def noise(stream_key, dims, width, limit, pieces=(), kind=jnp.bfloat16):
    result = jax.random.normal(stream_key, dims, jnp.float32) * width
    if len(pieces) > 0:
        result = shard_levels(stream_key, dims, pieces, -0.22, 0.18) * result
    return jnp.clip(result, min=-limit, max=limit).astype(kind)


def setup_inputs(seed: int = 0) -> dict:
    splits = jax.random.split(jax.random.key(seed), 7)
    velocity_u = noise(splits[0], (NY, NZ, NX), 1.0, 6.0, ((0, 16), (1, 32)))
    velocity_v = noise(splits[1], (NY, NZ, NX), 1.0, 6.0, ((0, 16), (1, 32)))
    velocity_w = noise(splits[2], (NY, NZ, NX), 1.0, 6.0, ((0, 16), (1, 32)))
    x_derivative = draw_x_derivative(jax.random.fold_in(splits[6], 71), 0)
    y_derivative = draw_y_derivative(jax.random.fold_in(splits[6], 71), 0)
    z_derivative = draw_z_derivative(jax.random.fold_in(splits[6], 71), 0)
    return dict(velocity_u=velocity_u, velocity_v=velocity_v, velocity_w=velocity_w, x_derivative=x_derivative, y_derivative=y_derivative, z_derivative=z_derivative)


def reference(velocity_u, velocity_v, velocity_w, x_derivative, y_derivative, z_derivative):
    block_count = N_PCOL
    block_width = NZ // block_count

    def plane_section(index):
        start = (index * block_width).astype(jnp.int32)
        u_part = lax.dynamic_slice_in_dim(velocity_u, start, block_width, 1)
        v_part = lax.dynamic_slice_in_dim(velocity_v, start, block_width, 1)
        u_dx = jnp.dot(u_part.reshape(NY * block_width, NX), x_derivative.T,
                       preferred_element_type=jnp.float32).reshape(NY, block_width, NX).astype(jnp.bfloat16)
        u_dy = jnp.dot(y_derivative, u_part.reshape(NY, block_width * NX),
                       preferred_element_type=jnp.float32).reshape(NY, block_width, NX)
        v_dy = jnp.dot(y_derivative, v_part.reshape(NY, block_width * NX),
                       preferred_element_type=jnp.float32).reshape(NY, block_width, NX)
        partial_div = u_dx.astype(jnp.float32) + v_dy
        advect = u_part.astype(jnp.float32) * u_dx.astype(jnp.float32) + v_part.astype(jnp.float32) * u_dy
        return partial_div, advect

    partial_div, advect = lax.map(plane_section, jnp.arange(block_count, dtype=jnp.int32))
    partial_div = jnp.transpose(partial_div, (1, 0, 2, 3)).reshape(NY, NZ, NX)
    advect = jnp.transpose(advect, (1, 0, 2, 3)).reshape(NY, NZ, NX)

    def line_section(index):
        u_plane = lax.dynamic_index_in_dim(velocity_u, index, 0, keepdims=False)
        w_plane = lax.dynamic_index_in_dim(velocity_w, index, 0, keepdims=False)
        part_plane = lax.dynamic_index_in_dim(partial_div, index, 0, keepdims=False)
        adv_plane = lax.dynamic_index_in_dim(advect, index, 0, keepdims=False)
        u_dz = jnp.dot(z_derivative, u_plane, preferred_element_type=jnp.float32)
        w_dz = jnp.dot(z_derivative, w_plane, preferred_element_type=jnp.float32)
        return part_plane + w_dz, -(adv_plane + w_plane.astype(jnp.float32) * u_dz)

    divergence, u_tendency = lax.map(line_section, jnp.arange(NY, dtype=jnp.int32))
    return jnp.transpose(u_tendency, (0, 2, 1)), jnp.transpose(divergence, (1, 2, 0))
```

```python
import jax
import jax.numpy as jnp
from jax import lax
from jax.sharding import PartitionSpec as P


def body(velocity_u, velocity_v, velocity_w, x_derivative, y_derivative, z_derivative):
    n_row = lax.axis_size("prow")
    n_col = lax.axis_size("pcol")
    y_loc, z_loc, x_full = velocity_u.shape
    x_loc = x_full // n_row
    y_full = y_loc * n_row
    y_sub = y_full // n_col
    z_full = z_loc * n_col
    f32 = jnp.float32

    dx_full = lax.all_gather(x_derivative, "pcol", axis=0, tiled=True)
    dz_full = lax.all_gather(z_derivative, "prow", axis=0, tiled=True)

    def to_ypen(a):
        s = a.reshape(y_loc, z_loc, n_row, x_loc).transpose(2, 0, 1, 3)
        s = lax.all_to_all(s, "prow", 0, 0, tiled=True)
        return s.reshape(y_full, z_loc * x_loc)

    def to_zpen(a):
        s = a.reshape(n_col, y_sub, z_loc, x_loc).transpose(0, 2, 1, 3)
        s = lax.all_to_all(s, "pcol", 0, 0, tiled=True)
        return s.reshape(z_full, y_sub * x_loc)

    u_y = to_ypen(velocity_u)
    v_y = to_ypen(velocity_v)
    w_y = to_ypen(velocity_w)
    u_dy = jnp.dot(y_derivative, u_y, preferred_element_type=f32)
    v_dy = jnp.dot(y_derivative, v_y, preferred_element_type=f32)
    vudy_z = to_zpen(v_y.astype(f32) * u_dy)
    u_z = to_zpen(u_y)
    w_z = to_zpen(w_y)
    u_dz = jnp.dot(dz_full, u_z, preferred_element_type=f32)
    w_dz = jnp.dot(dz_full, w_z, preferred_element_type=f32)
    w_dz_d = lax.all_to_all(w_dz.reshape(n_col, z_loc, y_sub, x_loc), "pcol", 0, 0, tiled=True)

    dx_full, w_dz_d, vudy_z, u_dz, u_z, w_z, v_dy = lax.optimization_barrier(
        (dx_full, w_dz_d, vudy_z, u_dz, u_z, w_z, v_dy))
    u_dx = lax.dot_general(
        velocity_u.reshape(y_loc * z_loc, x_full),
        dx_full,
        (((1,), (1,)), ((), ())),
        preferred_element_type=f32,
    ).astype(jnp.bfloat16)
    udx_y = to_ypen(u_dx.reshape(y_loc, z_loc, x_full))
    udx_z = to_zpen(udx_y)

    advect_z = u_z.astype(f32) * udx_z.astype(f32) + vudy_z
    tend_z = -(advect_z + w_z.astype(f32) * u_dz)
    u_tendency = tend_z.T.reshape(y_sub, x_loc, z_full)

    part_y = udx_y.astype(f32) + v_dy
    part_d = part_y.reshape(y_full, z_loc, x_loc).transpose(1, 2, 0)
    wdz_d = w_dz_d.transpose(1, 3, 0, 2).reshape(z_loc, x_loc, y_full)
    divergence = part_d + wdz_d
    return (u_tendency, divergence)


def solution(mesh):
    in_specs = (
        P("prow", "pcol", None),
        P("prow", "pcol", None),
        P("prow", "pcol", None),
        P("pcol", None),
        P(),
        P("prow", None),
    )
    out_specs = (P("pcol", "prow", None), P("pcol", "prow", None))
    return jax.shard_map(body, mesh=mesh, in_specs=in_specs, out_specs=out_specs, check_vma=False)
```

```python
import jax
import jax.numpy as jnp
from jax import lax
from jax.sharding import Mesh
from jax.sharding import PartitionSpec as P


ROW = ("x", "ylo", "core")
COL = ("z", "yhi")


def body(velocity_u, velocity_v, velocity_w, x_derivative, y_derivative, z_derivative):
    n_row = lax.axis_size(ROW)
    n_col = lax.axis_size(COL)
    y_loc, z_loc, x_full = velocity_u.shape
    x_loc = x_full // n_row
    y_full = y_loc * n_row
    y_sub = y_full // n_col
    z_full = z_loc * n_col
    f32 = jnp.float32

    dx_half = lax.all_gather(x_derivative, "yhi", axis=0, tiled=True)
    dx_full = lax.all_gather(dx_half, "z", axis=0, tiled=True)
    dz_full = lax.all_gather(z_derivative, ROW, axis=0, tiled=True)

    def to_ypen(a):
        s = a.reshape(y_loc, z_loc, n_row, x_loc).transpose(2, 0, 1, 3)
        s = lax.all_to_all(s, ROW, 0, 0, tiled=True)
        return s.reshape(y_full, z_loc * x_loc)

    def to_zpen(a):
        s = a.reshape(n_col, y_sub, z_loc, x_loc).transpose(0, 2, 1, 3)
        s = lax.all_to_all(s, COL, 0, 0, tiled=True)
        return s.reshape(z_full, y_sub * x_loc)

    u_y = to_ypen(velocity_u)
    v_y = to_ypen(velocity_v)
    w_y = to_ypen(velocity_w)
    u_dy = jnp.dot(y_derivative, u_y, preferred_element_type=f32)
    v_dy = jnp.dot(y_derivative, v_y, preferred_element_type=f32)
    vudy = v_y.astype(f32) * u_dy
    u_z = to_zpen(u_y)
    w_z = to_zpen(w_y)
    u_dz = jnp.dot(dz_full, u_z, preferred_element_type=f32)
    w_dz = jnp.dot(dz_full, w_z, preferred_element_type=f32)
    w_dz_d = lax.all_to_all(w_dz.reshape(n_col, z_loc, y_sub, x_loc), COL, 0, 0, tiled=True)

    dx_full, w_dz_d, vudy, u_dz, u_z, w_z, v_dy = lax.optimization_barrier(
        (dx_full, w_dz_d, vudy, u_dz, u_z, w_z, v_dy))
    u_dx = lax.dot_general(
        velocity_u.reshape(y_loc * z_loc, x_full),
        dx_full,
        (((1,), (1,)), ((), ())),
        preferred_element_type=f32,
    ).astype(jnp.bfloat16)
    udx_y = to_ypen(u_dx.reshape(y_loc, z_loc, x_full)).astype(f32)

    advect_z = to_zpen(u_y.astype(f32) * udx_y + vudy)
    tend_z = -(advect_z + w_z.astype(f32) * u_dz)
    u_tendency = tend_z.T.reshape(y_sub, x_loc, z_full)

    part_y = udx_y + v_dy
    part_d = part_y.reshape(y_full, z_loc, x_loc).transpose(1, 2, 0)
    wdz_d = w_dz_d.transpose(1, 3, 0, 2).reshape(z_loc, x_loc, y_full)
    divergence = part_d + wdz_d
    return (u_tendency, divergence)


def solution(mesh):
    sizes = [4, 2, 2, 16, 2]
    fine = Mesh(mesh.devices.reshape(sizes), ROW + COL)
    in_specs = (
        P(ROW, COL, None),
        P(ROW, COL, None),
        P(ROW, COL, None),
        P(COL, None),
        P(),
        P(ROW, None),
    )
    out_specs = (P(COL, ROW, None), P(COL, ROW, None))
    return jax.shard_map(body, mesh=fine, in_specs=in_specs, out_specs=out_specs, check_vma=False)
```

```python
import jax
import jax.numpy as jnp
from jax import lax
from jax.sharding import Mesh
from jax.sharding import PartitionSpec as P


ROW = ("x", "ylo", "core")
COL = ("zhi", "zlo", "yhi")


def body(velocity_u, velocity_v, velocity_w, x_derivative, y_derivative, z_derivative):
    n_row = lax.axis_size(ROW)
    n_col = lax.axis_size(COL)
    y_loc, z_loc, x_full = velocity_u.shape
    x_loc = x_full // n_row
    y_full = y_loc * n_row
    y_sub = y_full // n_col
    z_full = z_loc * n_col
    f32 = jnp.float32

    dx_full = x_derivative
    for axis in COL[::-1]:
        dx_full = lax.all_gather(dx_full, axis, axis=0, tiled=True)
    dz_full = z_derivative
    for axis in ROW[::-1]:
        dz_full = lax.all_gather(dz_full, axis, axis=0, tiled=True)

    def to_ypen(a):
        s = a.reshape(y_loc, z_loc, n_row, x_loc).transpose(2, 0, 1, 3)
        s = lax.all_to_all(s, ROW, 0, 0, tiled=True)
        return s.reshape(y_full, z_loc * x_loc)

    def to_zpen(a):
        s = a.reshape(n_col, y_sub, z_loc, x_loc).transpose(0, 2, 1, 3)
        s = lax.all_to_all(s, COL, 0, 0, tiled=True)
        return s.reshape(z_full, y_sub * x_loc)

    uvw = jnp.stack([velocity_u, velocity_v, velocity_w])
    uvw = uvw.reshape(3, y_loc, z_loc, n_row, x_loc).transpose(3, 0, 1, 2, 4)
    uvw = lax.all_to_all(uvw, ROW, 0, 0, tiled=True)
    u_y, v_y, w_y = (uvw[:, f].reshape(y_full, z_loc * x_loc) for f in range(3))
    u_dy = jnp.dot(y_derivative, u_y, preferred_element_type=f32)
    v_dy = jnp.dot(y_derivative, v_y, preferred_element_type=f32)
    vudy = v_y.astype(f32) * u_dy
    uw = jnp.stack([u_y, w_y]).reshape(2, n_col, y_sub, z_loc, x_loc).transpose(1, 0, 3, 2, 4)
    uw = lax.all_to_all(uw, COL, 0, 0, tiled=True)
    u_z, w_z = (uw[:, f].reshape(z_full, y_sub * x_loc) for f in range(2))
    u_dz = jnp.dot(dz_full, u_z, preferred_element_type=f32)
    w_dz = jnp.dot(dz_full, w_z, preferred_element_type=f32)
    w_dz_d = lax.all_to_all(w_dz.reshape(n_col, z_loc, y_sub, x_loc), COL, 0, 0, tiled=True)

    dx_full, w_dz_d, vudy, u_dz, u_z, w_z, v_dy = lax.optimization_barrier(
        (dx_full, w_dz_d, vudy, u_dz, u_z, w_z, v_dy))
    u_dx = lax.dot_general(
        velocity_u.reshape(y_loc * z_loc, x_full),
        dx_full,
        (((1,), (1,)), ((), ())),
        preferred_element_type=f32,
    ).astype(jnp.bfloat16)
    udx_y = to_ypen(u_dx.reshape(y_loc, z_loc, x_full)).astype(f32)

    advect_z = to_zpen(u_y.astype(f32) * udx_y + vudy)
    tend_z = -(advect_z + w_z.astype(f32) * u_dz)
    u_tendency = tend_z.T.reshape(y_sub, x_loc, z_full)

    part_y = udx_y + v_dy
    part_d = part_y.reshape(y_full, z_loc, x_loc).transpose(1, 2, 0)
    wdz_d = w_dz_d.transpose(1, 3, 0, 2).reshape(z_loc, x_loc, y_full)
    divergence = part_d + wdz_d
    return (u_tendency, divergence)


def solution(mesh):
    sizes = [4, 2, 2, 4, 4, 2]
    fine = Mesh(mesh.devices.reshape(sizes), ROW + COL)
    in_specs = (
        P(ROW, COL, None),
        P(ROW, COL, None),
        P(ROW, COL, None),
        P(COL, None),
        P(),
        P(ROW, None),
    )
    out_specs = (P(COL, ROW, None), P(COL, ROW, None))
    return jax.shard_map(body, mesh=fine, in_specs=in_specs, out_specs=out_specs, check_vma=False)
```

```python
import jax
import jax.numpy as jnp
from jax import lax
from jax.sharding import Mesh
from jax.sharding import PartitionSpec as P


ROW = ("x", "ylo", "core")
COL = ("z", "yhi")


def body(velocity_u, velocity_v, velocity_w, x_derivative, y_derivative, z_derivative):
    n_row = lax.axis_size(ROW)
    n_col = lax.axis_size(COL)
    y_loc, z_loc, x_full = velocity_u.shape
    x_loc = x_full // n_row
    y_full = y_loc * n_row
    y_sub = y_full // n_col
    z_full = z_loc * n_col
    f32 = jnp.float32

    dx_half = lax.all_gather(x_derivative, "yhi", axis=0, tiled=True)
    dx_full = lax.all_gather(dx_half, "z", axis=0, tiled=True)
    dz_full = lax.all_gather(z_derivative, ROW, axis=0, tiled=True)

    def to_ypen(a):
        s = a.reshape(y_loc, z_loc, n_row, x_loc).transpose(2, 0, 1, 3)
        s = lax.all_to_all(s, ROW, 0, 0, tiled=True)
        return s.reshape(y_full, z_loc * x_loc)

    def to_zpen(a):
        s = a.reshape(n_col, y_sub, z_loc, x_loc).transpose(0, 2, 1, 3)
        s = lax.all_to_all(s, COL, 0, 0, tiled=True)
        return s.reshape(z_full, y_sub * x_loc)

    uvw = jnp.stack([velocity_u, velocity_v, velocity_w])
    uvw = uvw.reshape(3, y_loc, z_loc, n_row, x_loc).transpose(3, 0, 1, 2, 4)
    uvw = lax.all_to_all(uvw, ROW, 0, 0, tiled=True)
    u_y, v_y, w_y = (uvw[:, f].reshape(y_full, z_loc * x_loc) for f in range(3))
    u_dy = jnp.dot(y_derivative, u_y, preferred_element_type=f32)
    v_dy = jnp.dot(y_derivative, v_y, preferred_element_type=f32)
    vudy = v_y.astype(f32) * u_dy
    uw = jnp.stack([u_y, w_y]).reshape(2, n_col, y_sub, z_loc, x_loc).transpose(1, 0, 3, 2, 4)
    uw = lax.all_to_all(uw, COL, 0, 0, tiled=True)
    u_z, w_z = (uw[:, f].reshape(z_full, y_sub * x_loc) for f in range(2))
    u_dz = jnp.dot(dz_full, u_z, preferred_element_type=f32)
    w_dz = jnp.dot(dz_full, w_z, preferred_element_type=f32)
    w_dz_d = lax.all_to_all(w_dz.reshape(n_col, z_loc, y_sub, x_loc), COL, 0, 0, tiled=True)

    dx_full, w_dz_d, vudy, u_dz, u_z, w_z, v_dy = lax.optimization_barrier(
        (dx_full, w_dz_d, vudy, u_dz, u_z, w_z, v_dy))
    u_dx = lax.dot_general(
        velocity_u.reshape(y_loc * z_loc, x_full),
        dx_full,
        (((1,), (1,)), ((), ())),
        preferred_element_type=f32,
    ).astype(jnp.bfloat16)
    udx_y = to_ypen(u_dx.reshape(y_loc, z_loc, x_full)).astype(f32)

    advect_z = to_zpen(u_y.astype(f32) * udx_y + vudy)
    tend_z = -(advect_z + w_z.astype(f32) * u_dz)
    u_tendency = tend_z.T.reshape(y_sub, x_loc, z_full)

    part_y = udx_y + v_dy
    part_d = part_y.reshape(y_full, z_loc, x_loc).transpose(1, 2, 0)
    wdz_d = w_dz_d.transpose(1, 3, 0, 2).reshape(z_loc, x_loc, y_full)
    divergence = part_d + wdz_d
    return (u_tendency, divergence)


def solution(mesh):
    sizes = [4, 2, 2, 16, 2]
    fine = Mesh(mesh.devices.reshape(sizes), ROW + COL)
    in_specs = (
        P(ROW, COL, None),
        P(ROW, COL, None),
        P(ROW, COL, None),
        P(COL, None),
        P(),
        P(ROW, None),
    )
    out_specs = (P(COL, ROW, None), P(COL, ROW, None))
    return jax.shard_map(body, mesh=fine, in_specs=in_specs, out_specs=out_specs, check_vma=False)
```

```python
import jax
import jax.numpy as jnp
from jax import lax
from jax.sharding import Mesh
from jax.sharding import PartitionSpec as P


ROW = ("x", "ylo", "core")
COL = ("z", "yhi")


def body(velocity_u, velocity_v, velocity_w, x_derivative, y_derivative, z_derivative):
    n_row = lax.axis_size(ROW)
    n_col = lax.axis_size(COL)
    y_loc, z_loc, x_full = velocity_u.shape
    x_loc = x_full // n_row
    y_full = y_loc * n_row
    y_sub = y_full // n_col
    z_full = z_loc * n_col
    f32 = jnp.float32

    dx_half = lax.all_gather(x_derivative, "yhi", axis=0, tiled=True)
    dx_full = lax.all_gather(dx_half, "z", axis=0, tiled=True)
    dz_full = lax.all_gather(z_derivative, ROW, axis=0, tiled=True)

    def to_ypen(a):
        s = a.reshape(y_loc, z_loc, n_row, x_loc).transpose(2, 0, 1, 3)
        s = lax.all_to_all(s, ROW, 0, 0, tiled=True)
        return s.reshape(y_full, z_loc * x_loc)

    def to_zpen(a):
        s = a.reshape(n_col, y_sub, z_loc, x_loc).transpose(0, 2, 1, 3)
        s = lax.all_to_all(s, COL, 0, 0, tiled=True)
        return s.reshape(z_full, y_sub * x_loc)

    uvw = jnp.stack([velocity_u, velocity_v, velocity_w])
    uvw = uvw.reshape(3, y_loc, z_loc, n_row, x_loc).transpose(3, 0, 1, 2, 4)
    uvw = lax.all_to_all(uvw, ROW, 0, 0, tiled=True)
    u_y, v_y, w_y = (uvw[:, f].reshape(y_full, z_loc * x_loc) for f in range(3))
    u_dy = jnp.dot(y_derivative, u_y, preferred_element_type=f32)
    v_dy = jnp.dot(y_derivative, v_y, preferred_element_type=f32)
    vudy = v_y.astype(f32) * u_dy
    uw = jnp.stack([u_y, w_y]).reshape(2, n_col, y_sub, z_loc, x_loc).transpose(1, 0, 3, 2, 4)
    uw = lax.all_to_all(uw, COL, 0, 0, tiled=True)
    u_z, w_z = (uw[:, f].reshape(z_full, y_sub * x_loc) for f in range(2))
    u_dz = jnp.dot(dz_full, u_z, preferred_element_type=f32)
    w_dz = jnp.dot(dz_full, w_z, preferred_element_type=f32)

    dx_full, w_dz, vudy, u_dz, u_z, w_z, v_dy = lax.optimization_barrier(
        (dx_full, w_dz, vudy, u_dz, u_z, w_z, v_dy))
    u_dx = lax.dot_general(
        velocity_u.reshape(y_loc * z_loc, x_full),
        dx_full,
        (((1,), (1,)), ((), ())),
        preferred_element_type=f32,
    ).astype(jnp.bfloat16)
    udx_y = to_ypen(u_dx.reshape(y_loc, z_loc, x_full)).astype(f32)

    advect = (u_y.astype(f32) * udx_y + vudy).reshape(n_col, y_sub, z_loc, x_loc).transpose(0, 2, 1, 3)
    both = jnp.stack([advect, w_dz.reshape(n_col, z_loc, y_sub, x_loc)], axis=1)
    both = lax.all_to_all(both, COL, 0, 0, tiled=True)
    advect_z = both[:, 0].reshape(z_full, y_sub * x_loc)
    w_dz_d = both[:, 1]
    tend_z = -(advect_z + w_z.astype(f32) * u_dz)
    u_tendency = tend_z.T.reshape(y_sub, x_loc, z_full)

    part_y = udx_y + v_dy
    part_d = part_y.reshape(y_full, z_loc, x_loc).transpose(1, 2, 0)
    wdz_d = w_dz_d.transpose(1, 3, 0, 2).reshape(z_loc, x_loc, y_full)
    divergence = part_d + wdz_d
    return (u_tendency, divergence)


def solution(mesh):
    sizes = [4, 2, 2, 16, 2]
    fine = Mesh(mesh.devices.reshape(sizes), ROW + COL)
    in_specs = (
        P(ROW, COL, None),
        P(ROW, COL, None),
        P(ROW, COL, None),
        P(COL, None),
        P(),
        P(ROW, None),
    )
    out_specs = (P(COL, ROW, None), P(COL, ROW, None))
    return jax.shard_map(body, mesh=fine, in_specs=in_specs, out_specs=out_specs, check_vma=False)
```

```python
import jax
import jax.numpy as jnp
from jax import lax
from jax.sharding import Mesh
from jax.sharding import PartitionSpec as P


ROW = ("x", "ylo", "core")
COL = ("z", "yhi")


def body(velocity_u, velocity_v, velocity_w, x_derivative, y_derivative, z_derivative):
    n_row = lax.axis_size(ROW)
    n_col = lax.axis_size(COL)
    y_loc, z_loc, x_full = velocity_u.shape
    x_loc = x_full // n_row
    y_full = y_loc * n_row
    y_sub = y_full // n_col
    z_full = z_loc * n_col
    f32 = jnp.float32

    dx_half = lax.all_gather(x_derivative, "yhi", axis=0, tiled=True)
    dx_full = lax.all_gather(dx_half, "z", axis=0, tiled=True)
    dz_full = lax.all_gather(z_derivative, ROW, axis=0, tiled=True)

    def to_ypen(a):
        s = a.reshape(y_loc, z_loc, n_row, x_loc).transpose(2, 0, 1, 3)
        s = lax.all_to_all(s, ROW, 0, 0, tiled=True)
        return s.reshape(y_full, z_loc * x_loc)

    def to_zpen(a):
        s = a.reshape(n_col, y_sub, z_loc, x_loc).transpose(0, 2, 1, 3)
        s = lax.all_to_all(s, COL, 0, 0, tiled=True)
        return s.reshape(z_full, y_sub * x_loc)

    uvw = jnp.stack([velocity_u, velocity_v, velocity_w])
    uvw = uvw.reshape(3, y_loc, z_loc, n_row, x_loc).transpose(3, 0, 1, 2, 4)
    uvw = lax.all_to_all(uvw, ROW, 0, 0, tiled=True)
    u_y, v_y, w_y = (uvw[:, f].reshape(y_full, z_loc * x_loc) for f in range(3))
    u_dy = jnp.dot(y_derivative, u_y, preferred_element_type=f32)
    v_dy = jnp.dot(y_derivative, v_y, preferred_element_type=f32)
    vudy = v_y.astype(f32) * u_dy
    uw = jnp.stack([u_y, w_y]).reshape(2, n_col, y_sub, z_loc, x_loc).transpose(1, 0, 3, 2, 4)
    uw = lax.all_to_all(uw, COL, 0, 0, tiled=True)
    u_z, w_z = (uw[:, f].reshape(z_full, y_sub * x_loc) for f in range(2))
    u_dz = jnp.dot(dz_full, u_z, preferred_element_type=f32)
    w_dz = jnp.dot(dz_full, w_z, preferred_element_type=f32)
    w_dz_d = lax.all_to_all(w_dz.reshape(n_col, z_loc, y_sub, x_loc), COL, 0, 0, tiled=True)

    dx_full, vudy, u_dz, u_z, w_z, v_dy, _ = lax.optimization_barrier(
        (dx_full, vudy, u_dz, u_z, w_z, v_dy, w_dz))
    u_dx = lax.dot_general(
        velocity_u.reshape(y_loc * z_loc, x_full),
        dx_full,
        (((1,), (1,)), ((), ())),
        preferred_element_type=f32,
    ).astype(jnp.bfloat16)
    udx_y = to_ypen(u_dx.reshape(y_loc, z_loc, x_full)).astype(f32)

    advect_z = to_zpen(u_y.astype(f32) * udx_y + vudy)
    tend_z = -(advect_z + w_z.astype(f32) * u_dz)
    u_tendency = tend_z.T.reshape(y_sub, x_loc, z_full)

    part_y = udx_y + v_dy
    part_d = part_y.reshape(y_full, z_loc, x_loc).transpose(1, 2, 0)
    wdz_d = w_dz_d.transpose(1, 3, 0, 2).reshape(z_loc, x_loc, y_full)
    divergence = part_d + wdz_d
    return (u_tendency, divergence)


def solution(mesh):
    sizes = [4, 2, 2, 16, 2]
    fine = Mesh(mesh.devices.reshape(sizes), ROW + COL)
    in_specs = (
        P(ROW, COL, None),
        P(ROW, COL, None),
        P(ROW, COL, None),
        P(COL, None),
        P(),
        P(ROW, None),
    )
    out_specs = (P(COL, ROW, None), P(COL, ROW, None))
    return jax.shard_map(body, mesh=fine, in_specs=in_specs, out_specs=out_specs, check_vma=False)
```

```python
import jax
import jax.numpy as jnp
from jax import lax
from jax.sharding import Mesh
from jax.sharding import PartitionSpec as P


ROW = ("x", "ylo", "core")
COL = ("z", "yhi")


def body(velocity_u, velocity_v, velocity_w, x_derivative, y_derivative, z_derivative):
    n_row = lax.axis_size(ROW)
    n_col = lax.axis_size(COL)
    y_loc, z_loc, x_full = velocity_u.shape
    x_loc = x_full // n_row
    y_full = y_loc * n_row
    y_sub = y_full // n_col
    z_full = z_loc * n_col
    f32 = jnp.float32

    dx_half = lax.all_gather(x_derivative, "yhi", axis=0, tiled=True)
    dx_full = lax.all_gather(dx_half, "z", axis=0, tiled=True)
    dz_full = lax.all_gather(z_derivative, ROW, axis=0, tiled=True)

    def to_ypen(a):
        s = a.reshape(y_loc, z_loc, n_row, x_loc).transpose(2, 0, 1, 3)
        s = lax.all_to_all(s, ROW, 0, 0, tiled=True)
        return s.reshape(y_full, z_loc * x_loc)

    def to_zpen(a):
        s = a.reshape(n_col, y_sub, z_loc, x_loc).transpose(0, 2, 1, 3)
        s = lax.all_to_all(s, COL, 0, 0, tiled=True)
        return s.reshape(z_full, y_sub * x_loc)

    uvw = jnp.stack([velocity_u, velocity_v, velocity_w])
    uvw = uvw.reshape(3, y_loc, z_loc, n_row, x_loc).transpose(3, 0, 1, 2, 4)
    uvw = lax.all_to_all(uvw, ROW, 0, 0, tiled=True)
    u_y, v_y, w_y = (uvw[:, f].reshape(y_full, z_loc * x_loc) for f in range(3))
    u_dy = jnp.dot(y_derivative, u_y, preferred_element_type=f32)
    v_dy = jnp.dot(y_derivative, v_y, preferred_element_type=f32)
    vudy = v_y.astype(f32) * u_dy
    uw = jnp.stack([u_y, w_y]).reshape(2, n_col, y_sub, z_loc, x_loc).transpose(1, 0, 3, 2, 4)
    uw = lax.all_to_all(uw, COL, 0, 0, tiled=True)
    u_z, w_z = (uw[:, f].reshape(z_full, y_sub * x_loc) for f in range(2))
    u_dz = jnp.dot(dz_full, u_z, preferred_element_type=f32)
    w_dz = jnp.dot(dz_full, w_z, preferred_element_type=f32)

    dx_full, vudy, u_dz, u_z, w_z, v_dy, _ = lax.optimization_barrier(
        (dx_full, vudy, u_dz, u_z, w_z, v_dy, w_dz))
    u_dx = lax.dot_general(
        velocity_u.reshape(y_loc * z_loc, x_full),
        dx_full,
        (((1,), (1,)), ((), ())),
        preferred_element_type=f32,
    ).astype(jnp.bfloat16)
    w_dz_d = lax.all_to_all(w_dz.reshape(n_col, z_loc, y_sub, x_loc), COL, 0, 0, tiled=True)
    udx_s = u_dx.reshape(y_loc, z_loc, n_row, x_loc).transpose(2, 0, 1, 3)
    udx_s, w_dz_d = lax.optimization_barrier((udx_s, w_dz_d))
    udx_y = lax.all_to_all(udx_s, ROW, 0, 0, tiled=True).reshape(y_full, z_loc * x_loc).astype(f32)

    advect_z = to_zpen(u_y.astype(f32) * udx_y + vudy)
    tend_z = -(advect_z + w_z.astype(f32) * u_dz)
    u_tendency = tend_z.T.reshape(y_sub, x_loc, z_full)

    part_y = udx_y + v_dy
    part_d = part_y.reshape(y_full, z_loc, x_loc).transpose(1, 2, 0)
    wdz_d = w_dz_d.transpose(1, 3, 0, 2).reshape(z_loc, x_loc, y_full)
    divergence = part_d + wdz_d
    return (u_tendency, divergence)


def solution(mesh):
    sizes = [4, 2, 2, 16, 2]
    fine = Mesh(mesh.devices.reshape(sizes), ROW + COL)
    in_specs = (
        P(ROW, COL, None),
        P(ROW, COL, None),
        P(ROW, COL, None),
        P(COL, None),
        P(),
        P(ROW, None),
    )
    out_specs = (P(COL, ROW, None), P(COL, ROW, None))
    return jax.shard_map(body, mesh=fine, in_specs=in_specs, out_specs=out_specs, check_vma=False)
```

```python
import jax
import jax.numpy as jnp
from jax import lax
from jax.sharding import Mesh
from jax.sharding import PartitionSpec as P


ROW = ("x", "ylo", "core")
COL = ("z", "yhi")


def body(velocity_u, velocity_v, velocity_w, x_derivative, y_derivative, z_derivative):
    n_row = lax.axis_size(ROW)
    n_col = lax.axis_size(COL)
    y_loc, z_loc, x_full = velocity_u.shape
    x_loc = x_full // n_row
    y_full = y_loc * n_row
    y_sub = y_full // n_col
    z_full = z_loc * n_col
    f32 = jnp.float32

    half = x_full // 2
    dx_cols = lax.dynamic_slice_in_dim(x_derivative, lax.axis_index("core") * half, half, 1)
    dx_half = lax.all_gather(dx_cols, "yhi", axis=0, tiled=True)
    dx_full = lax.all_gather(dx_half, "z", axis=0, tiled=True)
    dz_full = lax.all_gather(z_derivative, ROW, axis=0, tiled=True)

    def to_ypen(a):
        s = a.reshape(y_loc, z_loc, n_row, x_loc).transpose(2, 0, 1, 3)
        s = lax.all_to_all(s, ROW, 0, 0, tiled=True)
        return s.reshape(y_full, z_loc * x_loc)

    def to_zpen(a):
        s = a.reshape(n_col, y_sub, z_loc, x_loc).transpose(0, 2, 1, 3)
        s = lax.all_to_all(s, COL, 0, 0, tiled=True)
        return s.reshape(z_full, y_sub * x_loc)

    uvw = jnp.stack([velocity_u, velocity_v, velocity_w])
    uvw = uvw.reshape(3, y_loc, z_loc, n_row, x_loc).transpose(3, 0, 1, 2, 4)
    uvw = lax.all_to_all(uvw, ROW, 0, 0, tiled=True)
    u_y, v_y, w_y = (uvw[:, f].reshape(y_full, z_loc * x_loc) for f in range(3))
    u_dy = jnp.dot(y_derivative, u_y, preferred_element_type=f32)
    v_dy = jnp.dot(y_derivative, v_y, preferred_element_type=f32)
    vudy = v_y.astype(f32) * u_dy
    uw = jnp.stack([u_y, w_y]).reshape(2, n_col, y_sub, z_loc, x_loc).transpose(1, 0, 3, 2, 4)
    uw = lax.all_to_all(uw, COL, 0, 0, tiled=True)
    u_z, w_z = (uw[:, f].reshape(z_full, y_sub * x_loc) for f in range(2))
    dx_full, uw = lax.optimization_barrier((dx_full, uw))
    dx_full = lax.all_gather(dx_full, "core", axis=1, tiled=True)
    u_dz = jnp.dot(dz_full, u_z, preferred_element_type=f32)
    w_dz = jnp.dot(dz_full, w_z, preferred_element_type=f32)
    w_dz_d = lax.all_to_all(w_dz.reshape(n_col, z_loc, y_sub, x_loc), COL, 0, 0, tiled=True)

    dx_full, vudy, u_dz, u_z, w_z, v_dy, _ = lax.optimization_barrier(
        (dx_full, vudy, u_dz, u_z, w_z, v_dy, w_dz))
    u_dx = lax.dot_general(
        velocity_u.reshape(y_loc * z_loc, x_full),
        dx_full,
        (((1,), (1,)), ((), ())),
        preferred_element_type=f32,
    ).astype(jnp.bfloat16)
    udx_y = to_ypen(u_dx.reshape(y_loc, z_loc, x_full)).astype(f32)

    advect_z = to_zpen(u_y.astype(f32) * udx_y + vudy)
    tend_z = -(advect_z + w_z.astype(f32) * u_dz)
    u_tendency = tend_z.T.reshape(y_sub, x_loc, z_full)

    part_y = udx_y + v_dy
    part_d = part_y.reshape(y_full, z_loc, x_loc).transpose(1, 2, 0)
    wdz_d = w_dz_d.transpose(1, 3, 0, 2).reshape(z_loc, x_loc, y_full)
    divergence = part_d + wdz_d
    return (u_tendency, divergence)


def solution(mesh):
    sizes = [4, 2, 2, 16, 2]
    fine = Mesh(mesh.devices.reshape(sizes), ROW + COL)
    in_specs = (
        P(ROW, COL, None),
        P(ROW, COL, None),
        P(ROW, COL, None),
        P(COL, None),
        P(),
        P(ROW, None),
    )
    out_specs = (P(COL, ROW, None), P(COL, ROW, None))
    return jax.shard_map(body, mesh=fine, in_specs=in_specs, out_specs=out_specs, check_vma=False)
```

```python
import jax
import jax.numpy as jnp
from jax import lax
from jax.sharding import Mesh
from jax.sharding import PartitionSpec as P


ROW = ("x", "ylo", "core")
COL = ("z", "yhi")


def body(velocity_u, velocity_v, velocity_w, x_derivative, y_derivative, z_derivative):
    n_row = lax.axis_size(ROW)
    n_col = lax.axis_size(COL)
    y_loc, z_loc, x_full = velocity_u.shape
    x_loc = x_full // n_row
    y_full = y_loc * n_row
    y_sub = y_full // n_col
    z_full = z_loc * n_col
    f32 = jnp.float32

    half = x_full // 2
    dx_cols = lax.dynamic_slice_in_dim(x_derivative, lax.axis_index("core") * half, half, 1)
    dx_half = lax.all_gather(dx_cols, "yhi", axis=0, tiled=True)
    dx_full = lax.all_gather(dx_half, "z", axis=0, tiled=True)
    dz_full = lax.all_gather(z_derivative, ROW, axis=0, tiled=True)

    def to_ypen(a):
        s = a.reshape(y_loc, z_loc, n_row, x_loc).transpose(2, 0, 1, 3)
        s = lax.all_to_all(s, ROW, 0, 0, tiled=True)
        return s.reshape(y_full, z_loc * x_loc)

    def to_zpen(a):
        s = a.reshape(n_col, y_sub, z_loc, x_loc).transpose(0, 2, 1, 3)
        s = lax.all_to_all(s, COL, 0, 0, tiled=True)
        return s.reshape(z_full, y_sub * x_loc)

    uvw = jnp.stack([velocity_u, velocity_v, velocity_w])
    uvw = uvw.reshape(3, y_loc, z_loc, n_row, x_loc).transpose(3, 0, 1, 2, 4)
    uvw = lax.all_to_all(uvw, ROW, 0, 0, tiled=True)
    u_y, v_y, w_y = (uvw[:, f].reshape(y_full, z_loc * x_loc) for f in range(3))
    u_dy = jnp.dot(y_derivative, u_y, preferred_element_type=f32)
    v_dy = jnp.dot(y_derivative, v_y, preferred_element_type=f32)
    vudy = v_y.astype(f32) * u_dy
    uw = jnp.stack([u_y, w_y]).reshape(2, n_col, y_sub, z_loc, x_loc).transpose(1, 0, 3, 2, 4)
    uw = lax.all_to_all(uw, COL, 0, 0, tiled=True)
    u_z, w_z = (uw[:, f].reshape(z_full, y_sub * x_loc) for f in range(2))
    dx_full, uw = lax.optimization_barrier((dx_full, uw))
    dx_full = lax.all_gather(dx_full, "core", axis=1, tiled=True)
    u_dz = jnp.dot(dz_full, u_z, preferred_element_type=f32)
    w_dz = jnp.dot(dz_full, w_z, preferred_element_type=f32)
    w_dz_d = lax.all_to_all(w_dz.reshape(n_col, z_loc, y_sub, x_loc), COL, 0, 0, tiled=True)
    w_dz_d, dx_full = lax.optimization_barrier((w_dz_d, dx_full))

    dx_full, vudy, u_dz, u_z, w_z, v_dy, _ = lax.optimization_barrier(
        (dx_full, vudy, u_dz, u_z, w_z, v_dy, w_dz))
    u_dx = lax.dot_general(
        velocity_u.reshape(y_loc * z_loc, x_full),
        dx_full,
        (((1,), (1,)), ((), ())),
        preferred_element_type=f32,
    ).astype(jnp.bfloat16)
    udx_s = u_dx.reshape(y_loc, z_loc, n_row, x_loc).transpose(2, 0, 1, 3)
    udx_s, w_dz_d = lax.optimization_barrier((udx_s, w_dz_d))
    udx_y = lax.all_to_all(udx_s, ROW, 0, 0, tiled=True).reshape(y_full, z_loc * x_loc).astype(f32)

    advect_z = to_zpen(u_y.astype(f32) * udx_y + vudy)
    tend_z = -(advect_z + w_z.astype(f32) * u_dz)
    u_tendency = tend_z.T.reshape(y_sub, x_loc, z_full)

    part_y = udx_y + v_dy
    part_d = part_y.reshape(y_full, z_loc, x_loc).transpose(1, 2, 0)
    wdz_d = w_dz_d.transpose(1, 3, 0, 2).reshape(z_loc, x_loc, y_full)
    divergence = part_d + wdz_d
    return (u_tendency, divergence)


def solution(mesh):
    sizes = [4, 2, 2, 16, 2]
    fine = Mesh(mesh.devices.reshape(sizes), ROW + COL)
    in_specs = (
        P(ROW, COL, None),
        P(ROW, COL, None),
        P(ROW, COL, None),
        P(COL, None),
        P(),
        P(ROW, None),
    )
    out_specs = (P(COL, ROW, None), P(COL, ROW, None))
    return jax.shard_map(body, mesh=fine, in_specs=in_specs, out_specs=out_specs, check_vma=False)
```

```python
import jax
import jax.numpy as jnp
from jax import lax
from jax.sharding import Mesh
from jax.sharding import PartitionSpec as P


ROW = ("x", "ylo", "core")
COL = ("z", "yhi")


def body(velocity_u, velocity_v, velocity_w, x_derivative, y_derivative, z_derivative):
    n_row = lax.axis_size(ROW)
    n_col = lax.axis_size(COL)
    y_loc, z_loc, x_full = velocity_u.shape
    x_loc = x_full // n_row
    y_full = y_loc * n_row
    y_sub = y_full // n_col
    z_full = z_loc * n_col
    f32 = jnp.float32

    half = x_full // 2
    dx_cols = lax.dynamic_slice_in_dim(x_derivative, lax.axis_index("core") * half, half, 1)
    dx_half = lax.all_gather(dx_cols, "yhi", axis=0, tiled=True)
    dx_full = lax.all_gather(dx_half, "z", axis=0, tiled=True)
    dz_full = lax.all_gather(z_derivative, ROW, axis=0, tiled=True)

    def to_ypen(a):
        s = a.reshape(y_loc, z_loc, n_row, x_loc).transpose(2, 0, 1, 3)
        s = lax.all_to_all(s, ROW, 0, 0, tiled=True)
        return s.reshape(y_full, z_loc * x_loc)

    def to_zpen(a):
        s = a.reshape(n_col, y_sub, z_loc, x_loc).transpose(0, 2, 1, 3)
        s = lax.all_to_all(s, COL, 0, 0, tiled=True)
        return s.reshape(z_full, y_sub * x_loc)

    uvw = jnp.stack([velocity_u, velocity_v, velocity_w])
    uvw = uvw.reshape(3, y_loc, z_loc, n_row, x_loc).transpose(3, 0, 1, 2, 4)
    uvw = lax.all_to_all(uvw, ROW, 0, 0, tiled=True)
    u_y, v_y, w_y = (uvw[:, f].reshape(y_full, z_loc * x_loc) for f in range(3))
    u_dy = jnp.dot(y_derivative, u_y, preferred_element_type=f32)
    v_dy = jnp.dot(y_derivative, v_y, preferred_element_type=f32)
    vudy = v_y.astype(f32) * u_dy
    uw = jnp.stack([u_y, w_y]).reshape(2, n_col, y_sub, z_loc, x_loc).transpose(1, 0, 3, 2, 4)
    uw = lax.all_to_all(uw, COL, 0, 0, tiled=True)
    u_z, w_z = (uw[:, f].reshape(z_full, y_sub * x_loc) for f in range(2))
    dx_full, uw, vudy, v_dy = lax.optimization_barrier((dx_full, uw, vudy, v_dy))
    dx_full = lax.all_gather(dx_full, "core", axis=1, tiled=True)
    u_dz = jnp.dot(dz_full, u_z, preferred_element_type=f32)
    w_dz = jnp.dot(dz_full, w_z, preferred_element_type=f32)
    w_dz_d = lax.all_to_all(w_dz.reshape(n_col, z_loc, y_sub, x_loc), COL, 0, 0, tiled=True)

    dx_full, vudy, u_dz, u_z, w_z, v_dy, _ = lax.optimization_barrier(
        (dx_full, vudy, u_dz, u_z, w_z, v_dy, w_dz))
    u_dx = lax.dot_general(
        velocity_u.reshape(y_loc * z_loc, x_full),
        dx_full,
        (((1,), (1,)), ((), ())),
        preferred_element_type=f32,
    ).astype(jnp.bfloat16)
    udx_y = to_ypen(u_dx.reshape(y_loc, z_loc, x_full)).astype(f32)

    advect_z = to_zpen(u_y.astype(f32) * udx_y + vudy)
    tend_z = -(advect_z + w_z.astype(f32) * u_dz)
    u_tendency = tend_z.T.reshape(y_sub, x_loc, z_full)

    part_y = udx_y + v_dy
    part_d = part_y.reshape(y_full, z_loc, x_loc).transpose(1, 2, 0)
    wdz_d = w_dz_d.transpose(1, 3, 0, 2).reshape(z_loc, x_loc, y_full)
    divergence = part_d + wdz_d
    return (u_tendency, divergence)


def solution(mesh):
    sizes = [4, 2, 2, 16, 2]
    fine = Mesh(mesh.devices.reshape(sizes), ROW + COL)
    in_specs = (
        P(ROW, COL, None),
        P(ROW, COL, None),
        P(ROW, COL, None),
        P(COL, None),
        P(),
        P(ROW, None),
    )
    out_specs = (P(COL, ROW, None), P(COL, ROW, None))
    return jax.shard_map(body, mesh=fine, in_specs=in_specs, out_specs=out_specs, check_vma=False)
```
